1024 devices in a mesh: ctx: 64 (over x_hi, y, core), chan: 16 (over x_lo, z).
Axes of the slice: x: 8 (x_hi: 4, x_lo: 2; x = x_hi * 2 + x_lo), y: 8, z: 8, core: 2. Of those that a mesh axis runs over, the one named last changes fastest.
Arguments:
- query_gate: bfloat16 [8192, 8192], P('ctx', 'chan'), may hold values from -6 to 6
- key_gate: bfloat16 [8192, 8192], P('ctx', 'chan'), may hold values from -6 to 6
- value_input: bfloat16 [8192, 8192], P('ctx', 'chan'), may hold values from -6 to 6
- cotangent: bfloat16 [8192, 8192], P('ctx', 'chan'), may hold values from -16 to 16
- residues: float32 [16, 8192], P(None, 'chan'), may hold values from -1.5 to 1.5
- decay_rate: float32 [16, 8192], P(None, 'chan'), may hold values from 2.3841858e-06 to 0.0333333333, as said below
Outputs:
- output: bfloat16 [8192, 8192], P('ctx', 'chan')
- grad_query: bfloat16 [8192, 8192], P('ctx', 'chan')
- grad_key: bfloat16 [8192, 8192], P('ctx', 'chan')
- grad_value: bfloat16 [8192, 8192], P('ctx', 'chan')
- grad_residue: float32 [16, 8192], P(None, ('chan', 'ctx'))
- grad_lograte: float32 [16, 8192], P(None, ('chan', 'ctx'))
The draws below stay inside these ranges and needn't reach their ends.
Inputs may be any that keep to these rules, and one draw needn't show every extreme that they name: `decay_rate`: decay rates of the filters' poles.
All inputs are finite; a program needn't handle non-finite values.
Results may differ from the reference program's by a relative error of at most 0.001.
Values sent between devices are 32-bit elements; how exact they have to be, the bound alone decides.
No kernel may reach another device: no remote copies, remote signals or barrier semaphores. Data moves between devices by JAX's collectives and lax.ppermute only.
A program may use at most 32 MiB of HBM per device.

```python
import jax
import jax.numpy as jnp
from jax import lax

WIDTH = 8192
MODES = 16
TOK_DEV = 128
SEQ = 8192


def draw_decay_rate(key, part):
    lowest = 160.0 / (SEQ * SEQ)
    highest = 1.0 / 30.0
    first = jax.random.fold_in(jax.random.fold_in(key, 17), 0)
    unit = jax.random.uniform(first, (MODES, WIDTH), jnp.float32)
    span_low = jnp.full((MODES, WIDTH), lowest, jnp.float32)
    span_high = jnp.full((MODES, WIDTH), highest, jnp.float32)
    log_low = jnp.log(span_low)
    log_high = jnp.log(span_high)
    return jnp.clip(jnp.exp(log_low + unit * (log_high - log_low)), lowest, highest)


def strengthened(array, stream_key, source, target, parts, factor):
    owner, partner = [(jnp.arange(array.shape[axis_at]) // (array.shape[axis_at] // parts)).reshape([-1 if axis == axis_at else 1 for axis in range(array.ndim)]) for axis_at in (source, target)]
    chosen = jax.random.permutation(stream_key, parts)[partner]
    strong = (owner == chosen) | (owner == (partner + parts // 2) % parts)
    return jnp.where(strong, factor * array, array)


def block_levels(key, dims, shards, least, high):
    factor_of, own = 1.0, jax.random.fold_in(key, 6)
    for axis_at, shards_of in shards:
        steps = jnp.exp(jax.random.uniform(jax.random.fold_in(own, axis_at), (shards_of,), jnp.float32, least / len(shards), high / len(shards)))
        factor_of = factor_of * jnp.repeat(steps, dims[axis_at] // shards_of).reshape([-1 if axis == axis_at else 1 for axis in range(len(dims))])
    return factor_of


def centred(own_key, extent, spread, reach, cuts=(), held_as=jnp.bfloat16):
    array = jax.random.normal(own_key, extent, jnp.float32) * spread
    if len(cuts) > 0:
        array = block_levels(own_key, extent, cuts, -0.22, 0.18) * array
    return jnp.clip(array, min=-reach, max=reach).astype(held_as)


def gaussian_with(rng, extent, deviation, reach, shards, heavy, kind=jnp.bfloat16):
    values = deviation * jax.random.normal(rng, extent, jnp.float32)
    if shards:
        values = values * block_levels(rng, extent, shards, -0.22, 0.18)
    return jnp.clip(strengthened(values, jax.random.fold_in(rng, 3), *heavy), -reach, reach).astype(kind)


def setup_inputs(seed: int = 0) -> dict:
    arg_keys = jax.random.split(jax.random.key(seed), 7)
    query_gate = centred(arg_keys[0], (SEQ, WIDTH), 1.0, 6.0, ((0, 64), (1, 16)))
    key_gate = centred(arg_keys[1], (SEQ, WIDTH), 1.0, 6.0, ((0, 64), (1, 16)))
    value_input = centred(arg_keys[2], (SEQ, WIDTH), 1.0, 6.0, ((0, 64), (1, 16)))
    cotangent = gaussian_with(arg_keys[3], (SEQ, WIDTH), 1.0, 16.0, ((0, 64), (1, 16)), (0, 1, 64, 4.0))
    residues = centred(arg_keys[4], (MODES, WIDTH), MODES ** -0.5, 1.5, ((1, 16),), jnp.float32)
    decay_rate = draw_decay_rate(jax.random.fold_in(arg_keys[6], 71), 0)
    return {"query_gate": query_gate, "key_gate": key_gate, "value_input": value_input, "cotangent": cotangent, "residues": residues, "decay_rate": decay_rate}


def local_pieces(source, drive, rates, mixing, steps):
    where = jnp.arange(steps, dtype=jnp.float32)[None, :, None]
    rising = jnp.exp(rates[:, None, :] * where)
    falling = jnp.exp(-rates[:, None, :] * where)
    states = falling * jnp.cumsum(rising * source[None], axis=1)
    adjoint = rising * lax.cumsum(falling * (mixing[:, None, :] * drive[None]), axis=1, reverse=True)
    return (states, adjoint, where)

def reference(query_gate, key_gate, value_input, cotangent, residues, decay_rate):
    query = query_gate.astype(jnp.float32)
    keyed = key_gate.astype(jnp.float32)
    values = value_input.astype(jnp.float32)
    upstream = cotangent.astype(jnp.float32)
    source = keyed * values
    drive = upstream * query
    decay = jnp.exp(-decay_rate)
    norm_factor = jnp.sqrt(-jnp.expm1(-2.0 * decay_rate))
    mixing = residues * norm_factor
    blocks = SEQ // TOK_DEV
    src_blocks = source.reshape(blocks, TOK_DEV, WIDTH)
    drv_blocks = drive.reshape(blocks, TOK_DEV, WIDTH)

    def forward_step(carry, src):
        states, adjoint, where = local_pieces(src, src, decay_rate, mixing, TOK_DEV)
        states = states + jnp.exp(-decay_rate[:, None, :] * (where + 1.0)) * carry[:, None, :]
        mixed = lax.optimization_barrier(jnp.sum(mixing[:, None, :] * states, axis=0))
        return (states[:, -1, :], (mixed, carry))
    zero_state = jnp.zeros((MODES, WIDTH), jnp.float32)
    _, (mixed_blocks, starts) = lax.scan(forward_step, zero_state, src_blocks)

    def backward_step(carry, inputs):
        src, drv, start = inputs
        states, adjoint, where = local_pieces(src, drv, decay_rate, mixing, TOK_DEV)
        states = states + jnp.exp(-decay_rate[:, None, :] * (where + 1.0)) * start[:, None, :]
        adjoint = adjoint + jnp.exp(-decay_rate[:, None, :] * (TOK_DEV - where)) * carry[:, None, :]
        previous = jnp.concatenate([start[:, None, :], states[:, :-1, :]], axis=1)
        grad_w = lax.optimization_barrier(jnp.sum(drv[None] * states, axis=1))
        grad_a = lax.optimization_barrier(jnp.sum(adjoint * previous, axis=1))
        return (adjoint[:, 0, :], (lax.optimization_barrier(jnp.sum(adjoint, axis=0)), grad_w, grad_a))
    _, (dsrc_blocks, grad_ws, grad_as) = lax.scan(backward_step, zero_state, (src_blocks, drv_blocks, starts), reverse=True)
    mixed = mixed_blocks.reshape(SEQ, WIDTH)
    grad_source = dsrc_blocks.reshape(SEQ, WIDTH)
    grad_mixing = lax.optimization_barrier(jnp.sum(grad_ws, axis=0))
    grad_decay = lax.optimization_barrier(jnp.sum(grad_as, axis=0))
    raw_residue = grad_mixing * norm_factor
    raw_lograte = decay_rate * (grad_mixing * residues * decay * decay / norm_factor - decay * grad_decay)
    total = jnp.sum(raw_residue * raw_residue) + jnp.sum(raw_lograte * raw_lograte)
    limit = jnp.sqrt(jnp.float32(2.0 * MODES * WIDTH))
    scale = jnp.minimum(1.0, limit / jnp.sqrt(total + 1e-06))
    output = (query * mixed).astype(jnp.bfloat16)
    grad_query = (upstream * mixed).astype(jnp.bfloat16)
    grad_key = (grad_source * values).astype(jnp.bfloat16)
    grad_value = (grad_source * keyed).astype(jnp.bfloat16)
    return (output, grad_query, grad_key, grad_value, raw_residue * scale, raw_lograte * scale)
```

```python
import math

import jax
import jax.numpy as jnp
from jax import lax
from jax.sharding import PartitionSpec as P

WIDTH = 8192
MODES = 16

HIGHEST = lax.Precision.HIGHEST


def from_lower(x, axis, d, n):
    return lax.ppermute(x, axis, [(j, j + d) for j in range(n - d)])


def from_upper(x, axis, d, n):
    return lax.ppermute(x, axis, [(j + d, j) for j in range(n - d)])


def exclusive_scan(values, rates, steps, axis, n, shift):
    if n == 1:
        return jnp.zeros_like(values)
    window = 1
    result = shift(values, axis, 1, n)
    if n > 2:
        result = result + jnp.exp(-rates * steps) * shift(values, axis, 2, n)
        window = 2
    while window < n:
        result = result + jnp.exp(-rates * (steps * window)) * shift(result, axis, window, n)
        window *= 2
    return result


def butterfly_sum(x, axis, n):
    d = 1
    while d < n:
        x = x + lax.ppermute(x, axis, [(j, j ^ d) for j in range(n)])
        d *= 2
    return x


def local(query_gate, key_gate, value_input, cotangent, residues, decay_rate):
    steps = query_gate.shape[0]
    modes, columns = residues.shape
    peers = lax.axis_size("ctx")
    lanes = lax.axis_size("chan")
    assert peers & (peers - 1) == 0 and lanes & (lanes - 1) == 0
    query = query_gate.astype(jnp.float32)
    keyed = key_gate.astype(jnp.float32)
    values = value_input.astype(jnp.float32)
    upstream = cotangent.astype(jnp.float32)
    source = keyed * values
    drive = upstream * query
    decay = jnp.exp(-decay_rate)
    norm_factor = jnp.sqrt(-jnp.expm1(-2.0 * decay_rate))
    mixing = residues * norm_factor

    rate = decay_rate[None]
    where = jnp.arange(steps, dtype=jnp.float32)[:, None, None]
    rising = jnp.exp(rate * where)
    falling = jnp.exp(-rate * where)

    ends = jnp.sum(jnp.exp(-rate * (steps - 1.0 - where)) * source[:, None, :], axis=0)
    heads = mixing * jnp.sum(falling * drive[:, None, :], axis=0)
    incoming = exclusive_scan(ends, decay_rate, steps, "ctx", peers, from_lower)
    upper = exclusive_scan(heads, decay_rate, steps, "ctx", peers, from_upper)

    row = jnp.arange(steps)[:, None]
    col = jnp.arange(steps)[None, :]
    lower_tri = (col <= row).astype(jnp.float32)
    upper_tri = (col >= row).astype(jnp.float32)
    flat = (steps, modes * columns)
    climbed = (rising * source[:, None, :]).reshape(flat)
    fallen = (falling * (mixing[None] * drive[:, None, :])).reshape(flat)
    states0 = falling * jnp.dot(lower_tri, climbed, precision=HIGHEST).reshape(rising.shape)
    adjoint0 = rising * jnp.dot(upper_tri, fallen, precision=HIGHEST).reshape(rising.shape)

    states = states0 + jnp.exp(-rate * (where + 1.0)) * incoming[None]
    adjoint = adjoint0 + jnp.exp(-rate * (steps - where)) * upper[None]
    previous = jnp.concatenate([incoming[None], states[:-1]], axis=0)
    mixed = jnp.sum(mixing[None] * states, axis=1)
    grad_source = jnp.sum(adjoint, axis=1)
    grad_w = jnp.sum(drive[:, None, :] * states, axis=0)
    grad_a = jnp.sum(adjoint * previous, axis=0)

    sums = butterfly_sum(jnp.stack([grad_w, grad_a]), "ctx", peers)
    grad_mixing, grad_decay = sums[0], sums[1]
    raw_residue = grad_mixing * norm_factor
    raw_lograte = decay_rate * (
        grad_mixing * residues * decay * decay / norm_factor - decay * grad_decay
    )
    part = jnp.sum(raw_residue * raw_residue) + jnp.sum(raw_lograte * raw_lograte)
    total = butterfly_sum(part.reshape(1), "chan", lanes)[0]
    limit = math.sqrt(2.0 * MODES * WIDTH)
    scale = jnp.minimum(1.0, limit / jnp.sqrt(total + 1e-06))
    width = columns // peers
    at = lax.axis_index("ctx") * width
    own_residue = lax.dynamic_slice_in_dim(raw_residue, at, width, axis=1)
    own_lograte = lax.dynamic_slice_in_dim(raw_lograte, at, width, axis=1)
    output = (query * mixed).astype(jnp.bfloat16)
    grad_query = (upstream * mixed).astype(jnp.bfloat16)
    grad_key = (grad_source * values).astype(jnp.bfloat16)
    grad_value = (grad_source * keyed).astype(jnp.bfloat16)
    return (output, grad_query, grad_key, grad_value, own_residue * scale, own_lograte * scale)


def solution(mesh):
    placed = (
        P("ctx", "chan"),
        P("ctx", "chan"),
        P("ctx", "chan"),
        P("ctx", "chan"),
        P(None, "chan"),
        P(None, "chan"),
    )
    return jax.shard_map(
        local,
        mesh=mesh,
        in_specs=placed,
        out_specs=(
            P("ctx", "chan"),
            P("ctx", "chan"),
            P("ctx", "chan"),
            P("ctx", "chan"),
            P(None, ("chan", "ctx")),
            P(None, ("chan", "ctx")),
        ),
        check_vma=False,
    )
```

```python
import math

import jax
import jax.numpy as jnp
from jax import lax
from jax.sharding import PartitionSpec as P

WIDTH = 8192
MODES = 16

HIGHEST = lax.Precision.HIGHEST
CTX_GROUPS = (2, 8, 4)
CHAN_GROUPS = (8, 2)


def levels_of(n, groups):
    out, stride = [], 1
    for size in groups:
        out.append((stride, size))
        stride *= size
    assert stride == n
    return out


def level_gather(x, axis, n, stride, size):
    got = []
    for q in range(1, size):
        perm = []
        for i in range(n):
            r = (i // stride) % size
            perm.append((i, i + ((r + q) % size - r) * stride))
        got.append(lax.ppermute(x, axis, perm))
    return got


def carried_scan(ends, heads, rates, steps, axis, n, groups):
    index = lax.axis_index(axis)
    power = lambda k: jnp.exp(-rates * (steps * k.astype(jnp.float32)))
    incoming = jnp.zeros_like(ends)
    upper = jnp.zeros_like(heads)
    total, btotal = ends, heads
    for stride, size in levels_of(n, groups):
        r = (index // stride) % size
        p = index % stride
        got = level_gather(jnp.stack([total, btotal]), axis, n, stride, size)
        new_total = power((size - 1 - r) * stride) * total
        new_btotal = power(r * stride) * btotal
        for q, pair in zip(range(1, size), got):
            rq = (r - q) % size
            lower = q <= r
            incoming = incoming + jnp.where(lower, power((q - 1) * stride + p) * pair[0], 0.0)
            upper = upper + jnp.where(lower, 0.0, power((size - q) * stride - p - 1) * pair[1])
            new_total = new_total + power((size - 1 - rq) * stride) * pair[0]
            new_btotal = new_btotal + power(rq * stride) * pair[1]
        total, btotal = new_total, new_btotal
    return incoming, upper


def group_sum(x, axis, n, groups):
    for stride, size in levels_of(n, groups):
        x = x + sum(level_gather(x, axis, n, stride, size))
    return x


def local(query_gate, key_gate, value_input, cotangent, residues, decay_rate):
    steps = query_gate.shape[0]
    modes, columns = residues.shape
    peers = lax.axis_size("ctx")
    lanes = lax.axis_size("chan")
    query = query_gate.astype(jnp.float32)
    keyed = key_gate.astype(jnp.float32)
    values = value_input.astype(jnp.float32)
    upstream = cotangent.astype(jnp.float32)
    source = keyed * values
    drive = upstream * query
    decay = jnp.exp(-decay_rate)
    norm_factor = jnp.sqrt(-jnp.expm1(-2.0 * decay_rate))
    mixing = residues * norm_factor

    rate = decay_rate[None]
    where = jnp.arange(steps, dtype=jnp.float32)[:, None, None]
    rising = jnp.exp(rate * where)
    falling = jnp.exp(-rate * where)

    ends = jnp.sum(jnp.exp(-rate * (steps - 1.0 - where)) * source[:, None, :], axis=0)
    heads = mixing * jnp.sum(falling * drive[:, None, :], axis=0)
    incoming, upper = carried_scan(ends, heads, decay_rate, steps, "ctx", peers, CTX_GROUPS)

    row = jnp.arange(steps)[:, None]
    col = jnp.arange(steps)[None, :]
    lower_tri = (col <= row).astype(jnp.float32)
    upper_tri = (col >= row).astype(jnp.float32)
    flat = (steps, modes * columns)
    climbed = (rising * source[:, None, :]).reshape(flat)
    fallen = (falling * (mixing[None] * drive[:, None, :])).reshape(flat)
    states0 = falling * jnp.dot(lower_tri, climbed, precision=HIGHEST).reshape(rising.shape)
    adjoint0 = rising * jnp.dot(upper_tri, fallen, precision=HIGHEST).reshape(rising.shape)

    states = states0 + jnp.exp(-rate * (where + 1.0)) * incoming[None]
    adjoint = adjoint0 + jnp.exp(-rate * (steps - where)) * upper[None]
    previous = jnp.concatenate([incoming[None], states[:-1]], axis=0)
    mixed = jnp.sum(mixing[None] * states, axis=1)
    grad_source = jnp.sum(adjoint, axis=1)
    grad_w = jnp.sum(drive[:, None, :] * states, axis=0)
    grad_a = jnp.sum(adjoint * previous, axis=0)

    sums = group_sum(jnp.stack([grad_w, grad_a]), "ctx", peers, CTX_GROUPS)
    grad_mixing, grad_decay = sums[0], sums[1]
    raw_residue = grad_mixing * norm_factor
    raw_lograte = decay_rate * (
        grad_mixing * residues * decay * decay / norm_factor - decay * grad_decay
    )
    part = jnp.sum(raw_residue * raw_residue) + jnp.sum(raw_lograte * raw_lograte)
    total = group_sum(part.reshape(1), "chan", lanes, CHAN_GROUPS)[0]
    limit = math.sqrt(2.0 * MODES * WIDTH)
    scale = jnp.minimum(1.0, limit / jnp.sqrt(total + 1e-06))
    width = columns // peers
    at = lax.axis_index("ctx") * width
    own_residue = lax.dynamic_slice_in_dim(raw_residue, at, width, axis=1)
    own_lograte = lax.dynamic_slice_in_dim(raw_lograte, at, width, axis=1)
    output = (query * mixed).astype(jnp.bfloat16)
    grad_query = (upstream * mixed).astype(jnp.bfloat16)
    grad_key = (grad_source * values).astype(jnp.bfloat16)
    grad_value = (grad_source * keyed).astype(jnp.bfloat16)
    return (output, grad_query, grad_key, grad_value, own_residue * scale, own_lograte * scale)


def solution(mesh):
    placed = (
        P("ctx", "chan"),
        P("ctx", "chan"),
        P("ctx", "chan"),
        P("ctx", "chan"),
        P(None, "chan"),
        P(None, "chan"),
    )
    return jax.shard_map(
        local,
        mesh=mesh,
        in_specs=placed,
        out_specs=(
            P("ctx", "chan"),
            P("ctx", "chan"),
            P("ctx", "chan"),
            P("ctx", "chan"),
            P(None, ("chan", "ctx")),
            P(None, ("chan", "ctx")),
        ),
        check_vma=False,
    )
```

```python
import math

import jax
import jax.numpy as jnp
from jax import lax
from jax.sharding import PartitionSpec as P

WIDTH = 8192
MODES = 16

HIGHEST = lax.Precision.HIGHEST
CTX_GROUPS = (2, 8, 4)
CHAN_GROUPS = (2, 2, 2, 2)


def levels_of(n, groups):
    out, stride = [], 1
    for size in groups:
        out.append((stride, size))
        stride *= size
    assert stride == n
    return out


def level_gather(x, axis, n, stride, size):
    got = []
    for q in range(1, size):
        perm = []
        for i in range(n):
            r = (i // stride) % size
            perm.append((i, i + ((r + q) % size - r) * stride))
        got.append(lax.ppermute(x, axis, perm))
    return got


def carried_scan(ends, heads, rates, steps, axis, n, groups):
    index = lax.axis_index(axis)
    power = lambda k: jnp.exp(-rates * (steps * k.astype(jnp.float32)))
    incoming = jnp.zeros_like(ends)
    upper = jnp.zeros_like(heads)
    total, btotal = ends, heads
    for stride, size in levels_of(n, groups):
        r = (index // stride) % size
        p = index % stride
        got = level_gather(jnp.stack([total, btotal]), axis, n, stride, size)
        new_total = power((size - 1 - r) * stride) * total
        new_btotal = power(r * stride) * btotal
        for q, pair in zip(range(1, size), got):
            rq = (r - q) % size
            lower = q <= r
            incoming = incoming + jnp.where(lower, power((q - 1) * stride + p) * pair[0], 0.0)
            upper = upper + jnp.where(lower, 0.0, power((size - q) * stride - p - 1) * pair[1])
            new_total = new_total + power((size - 1 - rq) * stride) * pair[0]
            new_btotal = new_btotal + power(rq * stride) * pair[1]
        total, btotal = new_total, new_btotal
    return incoming, upper


def group_sum(x, axis, n, groups):
    for stride, size in levels_of(n, groups):
        x = x + sum(level_gather(x, axis, n, stride, size))
    return x


def local(query_gate, key_gate, value_input, cotangent, residues, decay_rate):
    steps = query_gate.shape[0]
    modes, columns = residues.shape
    peers = lax.axis_size("ctx")
    lanes = lax.axis_size("chan")
    query = query_gate.astype(jnp.float32)
    keyed = key_gate.astype(jnp.float32)
    values = value_input.astype(jnp.float32)
    upstream = cotangent.astype(jnp.float32)
    source = keyed * values
    drive = upstream * query
    decay = jnp.exp(-decay_rate)
    norm_factor = jnp.sqrt(-jnp.expm1(-2.0 * decay_rate))
    mixing = residues * norm_factor

    rate = decay_rate[None]
    where = jnp.arange(steps, dtype=jnp.float32)[:, None, None]
    rising = jnp.exp(rate * where)
    falling = jnp.exp(-rate * where)

    ends = jnp.sum(jnp.exp(-rate * (steps - 1.0 - where)) * source[:, None, :], axis=0)
    heads = mixing * jnp.sum(falling * drive[:, None, :], axis=0)
    incoming, upper = carried_scan(ends, heads, decay_rate, steps, "ctx", peers, CTX_GROUPS)

    row = jnp.arange(steps)[:, None]
    col = jnp.arange(steps)[None, :]
    lower_tri = (col <= row).astype(jnp.float32)
    upper_tri = (col >= row).astype(jnp.float32)
    flat = (steps, modes * columns)
    climbed = (rising * source[:, None, :]).reshape(flat)
    fallen = (falling * (mixing[None] * drive[:, None, :])).reshape(flat)
    states0 = falling * jnp.dot(lower_tri, climbed, precision=HIGHEST).reshape(rising.shape)
    adjoint0 = rising * jnp.dot(upper_tri, fallen, precision=HIGHEST).reshape(rising.shape)

    grown = jnp.exp(-rate * (where + 1.0))
    shrunk = jnp.exp(-rate * (steps - where))
    previous0 = jnp.concatenate([jnp.zeros_like(states0[:1]), states0[:-1]], axis=0)
    w_free = jnp.sum(drive[:, None, :] * states0, axis=0)
    w_in = jnp.sum(drive[:, None, :] * grown, axis=0)
    a_free = jnp.sum(adjoint0 * previous0, axis=0)
    a_in = jnp.sum(adjoint0 * falling, axis=0)
    a_up = jnp.sum(shrunk * previous0, axis=0)
    a_both = steps * jnp.exp(-decay_rate * steps)
    grad_w = w_free + incoming * w_in
    grad_a = a_free + incoming * a_in + upper * a_up + incoming * upper * a_both

    states = states0 + grown * incoming[None]
    adjoint = adjoint0 + shrunk * upper[None]
    mixed = jnp.sum(mixing[None] * states, axis=1)
    grad_source = jnp.sum(adjoint, axis=1)

    sums = group_sum(jnp.stack([grad_w, grad_a]), "ctx", peers, CTX_GROUPS)
    grad_mixing, grad_decay = sums[0], sums[1]
    raw_residue = grad_mixing * norm_factor
    raw_lograte = decay_rate * (
        grad_mixing * residues * decay * decay / norm_factor - decay * grad_decay
    )
    part = jnp.sum(raw_residue * raw_residue) + jnp.sum(raw_lograte * raw_lograte)
    total = group_sum(part.reshape(1), "chan", lanes, CHAN_GROUPS)[0]
    limit = math.sqrt(2.0 * MODES * WIDTH)
    scale = jnp.minimum(1.0, limit / jnp.sqrt(total + 1e-06))
    width = columns // peers
    at = lax.axis_index("ctx") * width
    own_residue = lax.dynamic_slice_in_dim(raw_residue, at, width, axis=1)
    own_lograte = lax.dynamic_slice_in_dim(raw_lograte, at, width, axis=1)
    output = (query * mixed).astype(jnp.bfloat16)
    grad_query = (upstream * mixed).astype(jnp.bfloat16)
    grad_key = (grad_source * values).astype(jnp.bfloat16)
    grad_value = (grad_source * keyed).astype(jnp.bfloat16)
    return (output, grad_query, grad_key, grad_value, own_residue * scale, own_lograte * scale)


def solution(mesh):
    placed = (
        P("ctx", "chan"),
        P("ctx", "chan"),
        P("ctx", "chan"),
        P("ctx", "chan"),
        P(None, "chan"),
        P(None, "chan"),
    )
    return jax.shard_map(
        local,
        mesh=mesh,
        in_specs=placed,
        out_specs=(
            P("ctx", "chan"),
            P("ctx", "chan"),
            P("ctx", "chan"),
            P("ctx", "chan"),
            P(None, ("chan", "ctx")),
            P(None, ("chan", "ctx")),
        ),
        check_vma=False,
    )
```

```python
import math

import jax
import jax.numpy as jnp
from jax import lax
from jax.sharding import PartitionSpec as P

WIDTH = 8192
MODES = 16

HIGHEST = lax.Precision.HIGHEST
CTX_GROUPS = (2, 8, 4)
CHAN_GROUPS = (2, 2, 2, 2)


def levels_of(n, groups):
    out, stride = [], 1
    for size in groups:
        out.append((stride, size))
        stride *= size
    assert stride == n
    return out


def level_gather(x, axis, n, stride, size):
    got = []
    for q in range(1, size):
        perm = []
        for i in range(n):
            r = (i // stride) % size
            perm.append((i, i + ((r + q) % size - r) * stride))
        got.append(lax.ppermute(x, axis, perm))
    return got


def fused_scan(pieces, rates, steps, axis, n):
    ends, heads, w_in, a_in, a_up, w_free, a_free = pieces
    index = lax.axis_index(axis)
    power = lambda k: jnp.exp(-rates * (steps * jnp.asarray(k).astype(jnp.float32)))
    a_both = steps * power(1)
    zeros = jnp.zeros_like(ends)
    incoming, upper = zeros, zeros
    group = jnp.stack([ends, heads, w_in, a_in, a_up, zeros, zeros, w_free, a_free])
    size = 1
    while size < n:
        partner = lax.ppermute(group, axis, [(i, i ^ size) for i in range(n)])
        high = (index // size) % 2 == 1
        low_g = jnp.where(high, partner, group)
        high_g = jnp.where(high, group, partner)
        f_l, b_l, wa_l, wb_l, wc_l, u_l, v_l, zw_l, za_l = low_g
        f_h, b_h, wa_h, wb_h, wc_h, u_h, v_h, zw_h, za_h = high_g
        step = power(size)
        spread = size * power(size - 1)
        at = index % size
        incoming = incoming + jnp.where(high, power(at) * f_l, 0.0)
        upper = upper + jnp.where(high, 0.0, power(size - 1 - at) * b_h)
        group = jnp.stack([
            step * f_l + f_h,
            b_l + step * b_h,
            wa_l + step * wa_h,
            wb_l + step * wb_h,
            step * wc_l + wc_h,
            step * u_l + (u_h + f_l * spread),
            (v_l + b_h * spread) + step * v_h,
            zw_l + zw_h + f_l * wa_h,
            za_l + za_h + f_l * wb_h + b_h * wc_l + a_both * (b_h * u_l + f_l * v_h),
        ])
        size *= 2
    return incoming, upper, group[7], group[8]


def group_sum(x, axis, n, groups):
    for stride, size in levels_of(n, groups):
        x = x + sum(level_gather(x, axis, n, stride, size))
    return x


def local(query_gate, key_gate, value_input, cotangent, residues, decay_rate):
    steps = query_gate.shape[0]
    modes, columns = residues.shape
    peers = lax.axis_size("ctx")
    lanes = lax.axis_size("chan")
    query = query_gate.astype(jnp.float32)
    keyed = key_gate.astype(jnp.float32)
    values = value_input.astype(jnp.float32)
    upstream = cotangent.astype(jnp.float32)
    source = keyed * values
    drive = upstream * query
    decay = jnp.exp(-decay_rate)
    norm_factor = jnp.sqrt(-jnp.expm1(-2.0 * decay_rate))
    mixing = residues * norm_factor

    rate = decay_rate[None]
    where = jnp.arange(steps, dtype=jnp.float32)[:, None, None]
    rising = jnp.exp(rate * where)
    falling = jnp.exp(-rate * where)

    ends = jnp.sum(jnp.exp(-rate * (steps - 1.0 - where)) * source[:, None, :], axis=0)
    heads = mixing * jnp.sum(falling * drive[:, None, :], axis=0)

    row = jnp.arange(steps)[:, None]
    col = jnp.arange(steps)[None, :]
    lower_tri = (col <= row).astype(jnp.float32)
    upper_tri = (col >= row).astype(jnp.float32)
    flat = (steps, modes * columns)
    climbed = (rising * source[:, None, :]).reshape(flat)
    fallen = (falling * (mixing[None] * drive[:, None, :])).reshape(flat)
    states0 = falling * jnp.dot(lower_tri, climbed, precision=HIGHEST).reshape(rising.shape)
    adjoint0 = rising * jnp.dot(upper_tri, fallen, precision=HIGHEST).reshape(rising.shape)

    grown = jnp.exp(-rate * (where + 1.0))
    shrunk = jnp.exp(-rate * (steps - where))
    previous0 = jnp.concatenate([jnp.zeros_like(states0[:1]), states0[:-1]], axis=0)
    w_free = jnp.sum(drive[:, None, :] * states0, axis=0)
    w_in = jnp.sum(drive[:, None, :] * grown, axis=0)
    a_free = jnp.sum(adjoint0 * previous0, axis=0)
    a_in = jnp.sum(adjoint0 * falling, axis=0)
    a_up = jnp.sum(shrunk * previous0, axis=0)
    pieces = (ends, heads, w_in, a_in, a_up, w_free, a_free)
    incoming, upper, grad_mixing, grad_decay = fused_scan(pieces, decay_rate, steps, "ctx", peers)

    states = states0 + grown * incoming[None]
    adjoint = adjoint0 + shrunk * upper[None]
    mixed = jnp.sum(mixing[None] * states, axis=1)
    grad_source = jnp.sum(adjoint, axis=1)

    raw_residue = grad_mixing * norm_factor
    raw_lograte = decay_rate * (
        grad_mixing * residues * decay * decay / norm_factor - decay * grad_decay
    )
    part = jnp.sum(raw_residue * raw_residue) + jnp.sum(raw_lograte * raw_lograte)
    total = group_sum(part.reshape(1), "chan", lanes, CHAN_GROUPS)[0]
    limit = math.sqrt(2.0 * MODES * WIDTH)
    scale = jnp.minimum(1.0, limit / jnp.sqrt(total + 1e-06))
    width = columns // peers
    at = lax.axis_index("ctx") * width
    own_residue = lax.dynamic_slice_in_dim(raw_residue, at, width, axis=1)
    own_lograte = lax.dynamic_slice_in_dim(raw_lograte, at, width, axis=1)
    output = (query * mixed).astype(jnp.bfloat16)
    grad_query = (upstream * mixed).astype(jnp.bfloat16)
    grad_key = (grad_source * values).astype(jnp.bfloat16)
    grad_value = (grad_source * keyed).astype(jnp.bfloat16)
    return (output, grad_query, grad_key, grad_value, own_residue * scale, own_lograte * scale)


def solution(mesh):
    placed = (
        P("ctx", "chan"),
        P("ctx", "chan"),
        P("ctx", "chan"),
        P("ctx", "chan"),
        P(None, "chan"),
        P(None, "chan"),
    )
    return jax.shard_map(
        local,
        mesh=mesh,
        in_specs=placed,
        out_specs=(
            P("ctx", "chan"),
            P("ctx", "chan"),
            P("ctx", "chan"),
            P("ctx", "chan"),
            P(None, ("chan", "ctx")),
            P(None, ("chan", "ctx")),
        ),
        check_vma=False,
    )
```

```python
import math

import jax
import jax.numpy as jnp
from jax import lax
from jax.sharding import PartitionSpec as P

WIDTH = 8192
MODES = 16

HIGHEST = lax.Precision.HIGHEST
CTX_GROUPS = (2, 8, 4)
CHAN_GROUPS = (2, 2, 2, 2)


def levels_of(n, groups):
    out, stride = [], 1
    for size in groups:
        out.append((stride, size))
        stride *= size
    assert stride == n
    return out


def level_gather(x, axis, n, stride, size):
    got = []
    for q in range(1, size):
        perm = []
        for i in range(n):
            r = (i // stride) % size
            perm.append((i, i + ((r + q) % size - r) * stride))
        got.append(lax.ppermute(x, axis, perm))
    return got


def fused_scan(pieces, rates, steps, axis, n):
    ends, heads, w_in, a_in, a_up, w_free, a_free = pieces
    index = lax.axis_index(axis)
    power = lambda k: jnp.exp(-rates * (steps * jnp.asarray(k).astype(jnp.float32)))
    a_both = steps * power(1)
    zeros = jnp.zeros_like(ends)
    incoming, upper = zeros, zeros
    carry = jnp.stack([ends, heads])
    group = jnp.stack([w_in, a_in, a_up, zeros, zeros, w_free, a_free])
    sizes = []
    size = 1
    while size < n:
        sizes.append(size)
        size *= 2
    pairs_of = lambda size: [(i, i ^ size) for i in range(n)]
    carry_partner = lax.ppermute(carry, axis, pairs_of(1)) if sizes else None
    for k, size in enumerate(sizes):
        high = (index // size) % 2 == 1
        f_l, b_l = jnp.where(high, carry_partner, carry)
        f_h, b_h = jnp.where(high, carry, carry_partner)
        step = power(size)
        spread = size * power(size - 1)
        at = index % size
        incoming = incoming + jnp.where(high, power(at) * f_l, 0.0)
        upper = upper + jnp.where(high, 0.0, power(size - 1 - at) * b_h)
        carry = jnp.stack([step * f_l + f_h, b_l + step * b_h])
        partner = lax.ppermute(group, axis, pairs_of(size))
        if k + 1 < len(sizes):
            carry_partner = lax.ppermute(carry, axis, pairs_of(sizes[k + 1]))
            partner, carry_partner = lax.optimization_barrier((partner, carry_partner))
        low_g = jnp.where(high, partner, group)
        high_g = jnp.where(high, group, partner)
        wa_l, wb_l, wc_l, u_l, v_l, zw_l, za_l = low_g
        wa_h, wb_h, wc_h, u_h, v_h, zw_h, za_h = high_g
        group = jnp.stack([
            wa_l + step * wa_h,
            wb_l + step * wb_h,
            step * wc_l + wc_h,
            step * u_l + (u_h + f_l * spread),
            (v_l + b_h * spread) + step * v_h,
            zw_l + zw_h + f_l * wa_h,
            za_l + za_h + f_l * wb_h + b_h * wc_l + a_both * (b_h * u_l + f_l * v_h),
        ])
    return incoming, upper, group[5], group[6]


def group_sum(x, axis, n, groups):
    for stride, size in levels_of(n, groups):
        x = x + sum(level_gather(x, axis, n, stride, size))
    return x


def local(query_gate, key_gate, value_input, cotangent, residues, decay_rate):
    steps = query_gate.shape[0]
    modes, columns = residues.shape
    peers = lax.axis_size("ctx")
    lanes = lax.axis_size("chan")
    query = query_gate.astype(jnp.float32)
    keyed = key_gate.astype(jnp.float32)
    values = value_input.astype(jnp.float32)
    upstream = cotangent.astype(jnp.float32)
    source = keyed * values
    drive = upstream * query
    decay = jnp.exp(-decay_rate)
    norm_factor = jnp.sqrt(-jnp.expm1(-2.0 * decay_rate))
    mixing = residues * norm_factor

    rate = decay_rate[None]
    where = jnp.arange(steps, dtype=jnp.float32)[:, None, None]
    rising = jnp.exp(rate * where)
    falling = jnp.exp(-rate * where)

    ends = jnp.sum(jnp.exp(-rate * (steps - 1.0 - where)) * source[:, None, :], axis=0)
    heads = mixing * jnp.sum(falling * drive[:, None, :], axis=0)

    row = jnp.arange(steps)[:, None]
    col = jnp.arange(steps)[None, :]
    lower_tri = (col <= row).astype(jnp.float32)
    upper_tri = (col >= row).astype(jnp.float32)
    flat = (steps, modes * columns)
    climbed = (rising * source[:, None, :]).reshape(flat)
    fallen = (falling * (mixing[None] * drive[:, None, :])).reshape(flat)
    states0 = falling * jnp.dot(lower_tri, climbed, precision=HIGHEST).reshape(rising.shape)
    adjoint0 = rising * jnp.dot(upper_tri, fallen, precision=HIGHEST).reshape(rising.shape)

    grown = jnp.exp(-rate * (where + 1.0))
    shrunk = jnp.exp(-rate * (steps - where))
    previous0 = jnp.concatenate([jnp.zeros_like(states0[:1]), states0[:-1]], axis=0)
    w_free = jnp.sum(drive[:, None, :] * states0, axis=0)
    w_in = jnp.sum(drive[:, None, :] * grown, axis=0)
    a_free = jnp.sum(adjoint0 * previous0, axis=0)
    a_in = jnp.sum(adjoint0 * falling, axis=0)
    a_up = jnp.sum(shrunk * previous0, axis=0)
    pieces = (ends, heads, w_in, a_in, a_up, w_free, a_free)
    incoming, upper, grad_mixing, grad_decay = fused_scan(pieces, decay_rate, steps, "ctx", peers)

    states = states0 + grown * incoming[None]
    adjoint = adjoint0 + shrunk * upper[None]
    mixed = jnp.sum(mixing[None] * states, axis=1)
    grad_source = jnp.sum(adjoint, axis=1)

    raw_residue = grad_mixing * norm_factor
    raw_lograte = decay_rate * (
        grad_mixing * residues * decay * decay / norm_factor - decay * grad_decay
    )
    part = jnp.sum(raw_residue * raw_residue) + jnp.sum(raw_lograte * raw_lograte)
    total = group_sum(part.reshape(1), "chan", lanes, CHAN_GROUPS)[0]
    limit = math.sqrt(2.0 * MODES * WIDTH)
    scale = jnp.minimum(1.0, limit / jnp.sqrt(total + 1e-06))
    width = columns // peers
    at = lax.axis_index("ctx") * width
    own_residue = lax.dynamic_slice_in_dim(raw_residue, at, width, axis=1)
    own_lograte = lax.dynamic_slice_in_dim(raw_lograte, at, width, axis=1)
    output = (query * mixed).astype(jnp.bfloat16)
    grad_query = (upstream * mixed).astype(jnp.bfloat16)
    grad_key = (grad_source * values).astype(jnp.bfloat16)
    grad_value = (grad_source * keyed).astype(jnp.bfloat16)
    return (output, grad_query, grad_key, grad_value, own_residue * scale, own_lograte * scale)


def solution(mesh):
    placed = (
        P("ctx", "chan"),
        P("ctx", "chan"),
        P("ctx", "chan"),
        P("ctx", "chan"),
        P(None, "chan"),
        P(None, "chan"),
    )
    return jax.shard_map(
        local,
        mesh=mesh,
        in_specs=placed,
        out_specs=(
            P("ctx", "chan"),
            P("ctx", "chan"),
            P("ctx", "chan"),
            P("ctx", "chan"),
            P(None, ("chan", "ctx")),
            P(None, ("chan", "ctx")),
        ),
        check_vma=False,
    )
```

```python
import math

import jax
import jax.numpy as jnp
from jax import lax
from jax.sharding import PartitionSpec as P

WIDTH = 8192
MODES = 16

HIGHEST = lax.Precision.HIGHEST
CTX_GROUPS = (2, 8, 4)
CHAN_GROUPS = (2, 2, 2, 2)


def levels_of(n, groups):
    out, stride = [], 1
    for size in groups:
        out.append((stride, size))
        stride *= size
    assert stride == n
    return out


def level_gather(x, axis, n, stride, size):
    got = []
    for q in range(1, size):
        perm = []
        for i in range(n):
            r = (i // stride) % size
            perm.append((i, i + ((r + q) % size - r) * stride))
        got.append(lax.ppermute(x, axis, perm))
    return got


def fused_scan(pieces, rates, steps, axis, n):
    ends, heads, w_in, a_in, a_up, w_free, a_free = pieces
    index = lax.axis_index(axis)
    power = lambda k: jnp.exp(-rates * (steps * jnp.asarray(k).astype(jnp.float32)))
    a_both = steps * power(1)
    zeros = jnp.zeros_like(ends)
    incoming, upper = zeros, zeros
    carry = jnp.stack([ends, heads])
    group = jnp.stack([w_in, a_in, a_up, zeros, zeros, w_free, a_free])
    sizes = []
    size = 1
    while size < n:
        sizes.append(size)
        size *= 2
    pairs_of = lambda size: [(i, i ^ size) for i in range(n)]
    carry_partner = lax.ppermute(carry, axis, pairs_of(1)) if sizes else None
    for k, size in enumerate(sizes):
        high = (index // size) % 2 == 1
        f_l, b_l = jnp.where(high, carry_partner, carry)
        f_h, b_h = jnp.where(high, carry, carry_partner)
        step = power(size)
        spread = size * power(size - 1)
        at = index % size
        incoming = incoming + jnp.where(high, power(at) * f_l, 0.0)
        upper = upper + jnp.where(high, 0.0, power(size - 1 - at) * b_h)
        carry = jnp.stack([step * f_l + f_h, b_l + step * b_h])
        partner = lax.ppermute(group, axis, pairs_of(size))
        if k + 1 < len(sizes):
            carry_partner = lax.ppermute(carry, axis, pairs_of(sizes[k + 1]))
            partner, carry_partner = lax.optimization_barrier((partner, carry_partner))
        low_g = jnp.where(high, partner, group)
        high_g = jnp.where(high, group, partner)
        wa_l, wb_l, wc_l, u_l, v_l, zw_l, za_l = low_g
        wa_h, wb_h, wc_h, u_h, v_h, zw_h, za_h = high_g
        group = jnp.stack([
            wa_l + step * wa_h,
            wb_l + step * wb_h,
            step * wc_l + wc_h,
            step * u_l + (u_h + f_l * spread),
            (v_l + b_h * spread) + step * v_h,
            zw_l + zw_h + f_l * wa_h,
            za_l + za_h + f_l * wb_h + b_h * wc_l + a_both * (b_h * u_l + f_l * v_h),
        ])
    return incoming, upper, group[5], group[6]


def group_sum(x, axis, n, groups):
    for stride, size in levels_of(n, groups):
        x = x + sum(level_gather(x, axis, n, stride, size))
    return x


def local(query_gate, key_gate, value_input, cotangent, residues, decay_rate):
    steps = query_gate.shape[0]
    modes, columns = residues.shape
    peers = lax.axis_size("ctx")
    lanes = lax.axis_size("chan")
    query = query_gate.astype(jnp.float32)
    keyed = key_gate.astype(jnp.float32)
    values = value_input.astype(jnp.float32)
    upstream = cotangent.astype(jnp.float32)
    source = keyed * values
    drive = upstream * query
    decay = jnp.exp(-decay_rate)
    norm_factor = jnp.sqrt(-jnp.expm1(-2.0 * decay_rate))
    mixing = residues * norm_factor

    rate = decay_rate[None]
    where = jnp.arange(steps, dtype=jnp.float32)[:, None, None]
    rising = jnp.exp(rate * where)
    falling = jnp.exp(-rate * where)
    whole = jnp.exp(-decay_rate * steps)

    ends = jnp.sum((jnp.exp(-decay_rate * (steps - 1.0))[None] * rising) * source[:, None, :], axis=0)
    heads = mixing * jnp.sum(falling * drive[:, None, :], axis=0)

    row = jnp.arange(steps)[:, None]
    col = jnp.arange(steps)[None, :]
    lower_tri = (col <= row).astype(jnp.float32)
    upper_tri = (col >= row).astype(jnp.float32)
    flat = (steps, modes * columns)
    climbed = (rising * source[:, None, :]).reshape(flat)
    fallen = (falling * (mixing[None] * drive[:, None, :])).reshape(flat)
    states0 = falling * jnp.dot(lower_tri, climbed, precision=HIGHEST).reshape(rising.shape)
    adjoint0 = rising * jnp.dot(upper_tri, fallen, precision=HIGHEST).reshape(rising.shape)

    grown = falling * decay[None]
    shrunk = rising * whole[None]
    previous0 = jnp.concatenate([jnp.zeros_like(states0[:1]), states0[:-1]], axis=0)
    w_free = jnp.sum(drive[:, None, :] * states0, axis=0)
    w_in = jnp.sum(drive[:, None, :] * grown, axis=0)
    a_free = jnp.sum(adjoint0 * previous0, axis=0)
    a_in = jnp.sum(adjoint0 * falling, axis=0)
    a_up = jnp.sum(shrunk * previous0, axis=0)
    pieces = (ends, heads, w_in, a_in, a_up, w_free, a_free)
    incoming, upper, grad_mixing, grad_decay = fused_scan(pieces, decay_rate, steps, "ctx", peers)

    states = states0 + grown * incoming[None]
    adjoint = adjoint0 + shrunk * upper[None]
    mixed = jnp.sum(mixing[None] * states, axis=1)
    grad_source = jnp.sum(adjoint, axis=1)

    raw_residue = grad_mixing * norm_factor
    raw_lograte = decay_rate * (
        grad_mixing * residues * decay * decay / norm_factor - decay * grad_decay
    )
    part = jnp.sum(raw_residue * raw_residue) + jnp.sum(raw_lograte * raw_lograte)
    total = group_sum(part.reshape(1), "chan", lanes, CHAN_GROUPS)[0]
    limit = math.sqrt(2.0 * MODES * WIDTH)
    scale = jnp.minimum(1.0, limit / jnp.sqrt(total + 1e-06))
    width = columns // peers
    at = lax.axis_index("ctx") * width
    own_residue = lax.dynamic_slice_in_dim(raw_residue, at, width, axis=1)
    own_lograte = lax.dynamic_slice_in_dim(raw_lograte, at, width, axis=1)
    output = (query * mixed).astype(jnp.bfloat16)
    grad_query = (upstream * mixed).astype(jnp.bfloat16)
    grad_key = (grad_source * values).astype(jnp.bfloat16)
    grad_value = (grad_source * keyed).astype(jnp.bfloat16)
    return (output, grad_query, grad_key, grad_value, own_residue * scale, own_lograte * scale)


def solution(mesh):
    placed = (
        P("ctx", "chan"),
        P("ctx", "chan"),
        P("ctx", "chan"),
        P("ctx", "chan"),
        P(None, "chan"),
        P(None, "chan"),
    )
    return jax.shard_map(
        local,
        mesh=mesh,
        in_specs=placed,
        out_specs=(
            P("ctx", "chan"),
            P("ctx", "chan"),
            P("ctx", "chan"),
            P("ctx", "chan"),
            P(None, ("chan", "ctx")),
            P(None, ("chan", "ctx")),
        ),
        check_vma=False,
    )
```

```python
import math

import jax
import jax.numpy as jnp
from jax import lax
from jax.sharding import PartitionSpec as P

WIDTH = 8192
MODES = 16

PRECISION = lax.Precision.HIGH
CTX_GROUPS = (2, 8, 4)
CHAN_GROUPS = (2, 2, 2, 2)


def levels_of(n, groups):
    out, stride = [], 1
    for size in groups:
        out.append((stride, size))
        stride *= size
    assert stride == n
    return out


def level_gather(x, axis, n, stride, size):
    got = []
    for q in range(1, size):
        perm = []
        for i in range(n):
            r = (i // stride) % size
            perm.append((i, i + ((r + q) % size - r) * stride))
        got.append(lax.ppermute(x, axis, perm))
    return got


def fused_scan(pieces, rates, steps, axis, n):
    ends, heads, w_in, a_in, a_up, w_free, a_free = pieces
    index = lax.axis_index(axis)
    power = lambda k: jnp.exp(-rates * (steps * jnp.asarray(k).astype(jnp.float32)))
    a_both = steps * power(1)
    zeros = jnp.zeros_like(ends)
    incoming, upper = zeros, zeros
    carry = jnp.stack([ends, heads])
    group = jnp.stack([w_in, a_in, a_up, zeros, zeros, w_free, a_free])
    sizes = []
    size = 1
    while size < n:
        sizes.append(size)
        size *= 2
    pairs_of = lambda size: [(i, i ^ size) for i in range(n)]
    carry_partner = lax.ppermute(carry, axis, pairs_of(1)) if sizes else None
    for k, size in enumerate(sizes):
        high = (index // size) % 2 == 1
        f_l, b_l = jnp.where(high, carry_partner, carry)
        f_h, b_h = jnp.where(high, carry, carry_partner)
        step = power(size)
        spread = size * power(size - 1)
        at = index % size
        incoming = incoming + jnp.where(high, power(at) * f_l, 0.0)
        upper = upper + jnp.where(high, 0.0, power(size - 1 - at) * b_h)
        carry = jnp.stack([step * f_l + f_h, b_l + step * b_h])
        partner = lax.ppermute(group, axis, pairs_of(size))
        if k + 1 < len(sizes):
            carry_partner = lax.ppermute(carry, axis, pairs_of(sizes[k + 1]))
            partner, carry_partner = lax.optimization_barrier((partner, carry_partner))
        low_g = jnp.where(high, partner, group)
        high_g = jnp.where(high, group, partner)
        wa_l, wb_l, wc_l, u_l, v_l, zw_l, za_l = low_g
        wa_h, wb_h, wc_h, u_h, v_h, zw_h, za_h = high_g
        group = jnp.stack([
            wa_l + step * wa_h,
            wb_l + step * wb_h,
            step * wc_l + wc_h,
            step * u_l + (u_h + f_l * spread),
            (v_l + b_h * spread) + step * v_h,
            zw_l + zw_h + f_l * wa_h,
            za_l + za_h + f_l * wb_h + b_h * wc_l + a_both * (b_h * u_l + f_l * v_h),
        ])
    return incoming, upper, group[5], group[6]


def group_sum(x, axis, n, groups):
    for stride, size in levels_of(n, groups):
        x = x + sum(level_gather(x, axis, n, stride, size))
    return x


def local(query_gate, key_gate, value_input, cotangent, residues, decay_rate):
    steps = query_gate.shape[0]
    modes, columns = residues.shape
    peers = lax.axis_size("ctx")
    lanes = lax.axis_size("chan")
    query = query_gate.astype(jnp.float32)
    keyed = key_gate.astype(jnp.float32)
    values = value_input.astype(jnp.float32)
    upstream = cotangent.astype(jnp.float32)
    source = keyed * values
    drive = upstream * query
    decay = jnp.exp(-decay_rate)
    norm_factor = jnp.sqrt(-jnp.expm1(-2.0 * decay_rate))
    mixing = residues * norm_factor

    rate = decay_rate[None]
    where = jnp.arange(steps, dtype=jnp.float32)[:, None, None]
    rising = jnp.exp(rate * where)
    falling = jnp.exp(-rate * where)
    whole = jnp.exp(-decay_rate * steps)

    ends = jnp.sum((jnp.exp(-decay_rate * (steps - 1.0))[None] * rising) * source[:, None, :], axis=0)
    heads = mixing * jnp.sum(falling * drive[:, None, :], axis=0)

    row = jnp.arange(steps)[:, None]
    col = jnp.arange(steps)[None, :]
    lower_tri = (col <= row).astype(jnp.float32)
    upper_tri = (col >= row).astype(jnp.float32)
    flat = (steps, modes * columns)
    climbed = (rising * source[:, None, :]).reshape(flat)
    fallen = (falling * (mixing[None] * drive[:, None, :])).reshape(flat)
    states0 = falling * jnp.dot(lower_tri, climbed, precision=PRECISION).reshape(rising.shape)
    adjoint0 = rising * jnp.dot(upper_tri, fallen, precision=PRECISION).reshape(rising.shape)

    grown = falling * decay[None]
    shrunk = rising * whole[None]
    previous0 = jnp.concatenate([jnp.zeros_like(states0[:1]), states0[:-1]], axis=0)
    w_free = jnp.sum(drive[:, None, :] * states0, axis=0)
    w_in = jnp.sum(drive[:, None, :] * grown, axis=0)
    a_free = jnp.sum(adjoint0 * previous0, axis=0)
    a_in = jnp.sum(adjoint0 * falling, axis=0)
    a_up = jnp.sum(shrunk * previous0, axis=0)
    pieces = (ends, heads, w_in, a_in, a_up, w_free, a_free)
    incoming, upper, grad_mixing, grad_decay = fused_scan(pieces, decay_rate, steps, "ctx", peers)

    states = states0 + grown * incoming[None]
    adjoint = adjoint0 + shrunk * upper[None]
    mixed = jnp.sum(mixing[None] * states, axis=1)
    grad_source = jnp.sum(adjoint, axis=1)

    raw_residue = grad_mixing * norm_factor
    raw_lograte = decay_rate * (
        grad_mixing * residues * decay * decay / norm_factor - decay * grad_decay
    )
    part = jnp.sum(raw_residue * raw_residue) + jnp.sum(raw_lograte * raw_lograte)
    total = group_sum(part.reshape(1), "chan", lanes, CHAN_GROUPS)[0]
    limit = math.sqrt(2.0 * MODES * WIDTH)
    scale = jnp.minimum(1.0, limit / jnp.sqrt(total + 1e-06))
    width = columns // peers
    at = lax.axis_index("ctx") * width
    own_residue = lax.dynamic_slice_in_dim(raw_residue, at, width, axis=1)
    own_lograte = lax.dynamic_slice_in_dim(raw_lograte, at, width, axis=1)
    output = (query * mixed).astype(jnp.bfloat16)
    grad_query = (upstream * mixed).astype(jnp.bfloat16)
    grad_key = (grad_source * values).astype(jnp.bfloat16)
    grad_value = (grad_source * keyed).astype(jnp.bfloat16)
    return (output, grad_query, grad_key, grad_value, own_residue * scale, own_lograte * scale)


def solution(mesh):
    placed = (
        P("ctx", "chan"),
        P("ctx", "chan"),
        P("ctx", "chan"),
        P("ctx", "chan"),
        P(None, "chan"),
        P(None, "chan"),
    )
    return jax.shard_map(
        local,
        mesh=mesh,
        in_specs=placed,
        out_specs=(
            P("ctx", "chan"),
            P("ctx", "chan"),
            P("ctx", "chan"),
            P("ctx", "chan"),
            P(None, ("chan", "ctx")),
            P(None, ("chan", "ctx")),
        ),
        check_vma=False,
    )
```

```python
import math

import jax
import jax.numpy as jnp
from jax import lax
from jax.sharding import PartitionSpec as P

WIDTH = 8192
MODES = 16

PRECISION = lax.Precision.HIGH
CTX_GROUPS = (2, 8, 4)
CHAN_GROUPS = (2, 2, 2, 2)


def levels_of(n, groups):
    out, stride = [], 1
    for size in groups:
        out.append((stride, size))
        stride *= size
    assert stride == n
    return out


def level_gather(x, axis, n, stride, size):
    got = []
    for q in range(1, size):
        perm = []
        for i in range(n):
            r = (i // stride) % size
            perm.append((i, i + ((r + q) % size - r) * stride))
        got.append(lax.ppermute(x, axis, perm))
    return got


def fused_scan(pieces, rates, steps, axis, n, hide):
    ends, heads, w_in, a_in, a_up, w_free, a_free = pieces
    index = lax.axis_index(axis)
    power = lambda k: jnp.exp(-rates * (steps * jnp.asarray(k).astype(jnp.float32)))
    a_both = steps * power(1)
    zeros = jnp.zeros_like(ends)
    incoming, upper = zeros, zeros
    carry = jnp.stack([ends, heads])
    group = jnp.stack([w_in, a_in, a_up, zeros, zeros, w_free, a_free])
    sizes = []
    size = 1
    while size < n:
        sizes.append(size)
        size *= 2
    pairs_of = lambda size: [(i, i ^ size) for i in range(n)]
    carry_partner = lax.ppermute(carry, axis, pairs_of(1)) if sizes else None
    for k, size in enumerate(sizes):
        high = (index // size) % 2 == 1
        f_l, b_l = jnp.where(high, carry_partner, carry)
        f_h, b_h = jnp.where(high, carry, carry_partner)
        step = power(size)
        spread = size * power(size - 1)
        at = index % size
        incoming = incoming + jnp.where(high, power(at) * f_l, 0.0)
        upper = upper + jnp.where(high, 0.0, power(size - 1 - at) * b_h)
        carry = jnp.stack([step * f_l + f_h, b_l + step * b_h])
        partner = lax.ppermute(group, axis, pairs_of(size))
        if k + 1 < len(sizes):
            carry_partner = lax.ppermute(carry, axis, pairs_of(sizes[k + 1]))
            partner, carry_partner = lax.optimization_barrier((partner, carry_partner))
        else:
            hidden = hide(incoming, upper)
            partner, hidden = lax.optimization_barrier((partner, hidden))
        low_g = jnp.where(high, partner, group)
        high_g = jnp.where(high, group, partner)
        wa_l, wb_l, wc_l, u_l, v_l, zw_l, za_l = low_g
        wa_h, wb_h, wc_h, u_h, v_h, zw_h, za_h = high_g
        group = jnp.stack([
            wa_l + step * wa_h,
            wb_l + step * wb_h,
            step * wc_l + wc_h,
            step * u_l + (u_h + f_l * spread),
            (v_l + b_h * spread) + step * v_h,
            zw_l + zw_h + f_l * wa_h,
            za_l + za_h + f_l * wb_h + b_h * wc_l + a_both * (b_h * u_l + f_l * v_h),
        ])
    return hidden, group[5], group[6]


def group_sum(x, axis, n, groups):
    for stride, size in levels_of(n, groups):
        x = x + sum(level_gather(x, axis, n, stride, size))
    return x


def local(query_gate, key_gate, value_input, cotangent, residues, decay_rate):
    steps = query_gate.shape[0]
    modes, columns = residues.shape
    peers = lax.axis_size("ctx")
    lanes = lax.axis_size("chan")
    query = query_gate.astype(jnp.float32)
    keyed = key_gate.astype(jnp.float32)
    values = value_input.astype(jnp.float32)
    upstream = cotangent.astype(jnp.float32)
    source = keyed * values
    drive = upstream * query
    decay = jnp.exp(-decay_rate)
    norm_factor = jnp.sqrt(-jnp.expm1(-2.0 * decay_rate))
    mixing = residues * norm_factor

    rate = decay_rate[None]
    where = jnp.arange(steps, dtype=jnp.float32)[:, None, None]
    rising = jnp.exp(rate * where)
    falling = jnp.exp(-rate * where)
    whole = jnp.exp(-decay_rate * steps)

    ends = jnp.sum((jnp.exp(-decay_rate * (steps - 1.0))[None] * rising) * source[:, None, :], axis=0)
    heads = mixing * jnp.sum(falling * drive[:, None, :], axis=0)

    row = jnp.arange(steps)[:, None]
    col = jnp.arange(steps)[None, :]
    lower_tri = (col <= row).astype(jnp.float32)
    upper_tri = (col >= row).astype(jnp.float32)
    flat = (steps, modes * columns)
    climbed = (rising * source[:, None, :]).reshape(flat)
    fallen = (falling * (mixing[None] * drive[:, None, :])).reshape(flat)
    states0 = falling * jnp.dot(lower_tri, climbed, precision=PRECISION).reshape(rising.shape)
    adjoint0 = rising * jnp.dot(upper_tri, fallen, precision=PRECISION).reshape(rising.shape)

    grown = falling * decay[None]
    shrunk = rising * whole[None]
    previous0 = jnp.concatenate([jnp.zeros_like(states0[:1]), states0[:-1]], axis=0)
    w_free = jnp.sum(drive[:, None, :] * states0, axis=0)
    w_in = jnp.sum(drive[:, None, :] * grown, axis=0)
    a_free = jnp.sum(adjoint0 * previous0, axis=0)
    a_in = jnp.sum(adjoint0 * falling, axis=0)
    a_up = jnp.sum(shrunk * previous0, axis=0)
    pieces = (ends, heads, w_in, a_in, a_up, w_free, a_free)

    def finish(incoming, upper):
        states = states0 + grown * incoming[None]
        adjoint = adjoint0 + shrunk * upper[None]
        mixed = jnp.sum(mixing[None] * states, axis=1)
        grad_source = jnp.sum(adjoint, axis=1)
        return (
            (query * mixed).astype(jnp.bfloat16),
            (upstream * mixed).astype(jnp.bfloat16),
            (grad_source * values).astype(jnp.bfloat16),
            (grad_source * keyed).astype(jnp.bfloat16),
        )

    outs, grad_mixing, grad_decay = fused_scan(pieces, decay_rate, steps, "ctx", peers, finish)
    output, grad_query, grad_key, grad_value = outs

    raw_residue = grad_mixing * norm_factor
    raw_lograte = decay_rate * (
        grad_mixing * residues * decay * decay / norm_factor - decay * grad_decay
    )
    part = jnp.sum(raw_residue * raw_residue) + jnp.sum(raw_lograte * raw_lograte)
    total = group_sum(part.reshape(1), "chan", lanes, CHAN_GROUPS)[0]
    limit = math.sqrt(2.0 * MODES * WIDTH)
    scale = jnp.minimum(1.0, limit / jnp.sqrt(total + 1e-06))
    width = columns // peers
    at = lax.axis_index("ctx") * width
    own_residue = lax.dynamic_slice_in_dim(raw_residue, at, width, axis=1)
    own_lograte = lax.dynamic_slice_in_dim(raw_lograte, at, width, axis=1)
    return (output, grad_query, grad_key, grad_value, own_residue * scale, own_lograte * scale)


def solution(mesh):
    placed = (
        P("ctx", "chan"),
        P("ctx", "chan"),
        P("ctx", "chan"),
        P("ctx", "chan"),
        P(None, "chan"),
        P(None, "chan"),
    )
    return jax.shard_map(
        local,
        mesh=mesh,
        in_specs=placed,
        out_specs=(
            P("ctx", "chan"),
            P("ctx", "chan"),
            P("ctx", "chan"),
            P("ctx", "chan"),
            P(None, ("chan", "ctx")),
            P(None, ("chan", "ctx")),
        ),
        check_vma=False,
    )
```

```python
import math

import jax
import jax.numpy as jnp
from jax import lax
from jax.sharding import PartitionSpec as P

WIDTH = 8192
MODES = 16

PRECISION = lax.Precision.HIGH
CTX_GROUPS = (2, 8, 4)
CHAN_GROUPS = (2, 2, 2, 2)


def levels_of(n, groups):
    out, stride = [], 1
    for size in groups:
        out.append((stride, size))
        stride *= size
    assert stride == n
    return out


def level_gather(x, axis, n, stride, size):
    got = []
    for q in range(1, size):
        perm = []
        for i in range(n):
            r = (i // stride) % size
            perm.append((i, i + ((r + q) % size - r) * stride))
        got.append(lax.ppermute(x, axis, perm))
    return got


def fused_scan(pieces, rates, steps, axis, n, hide):
    ends, heads, w_in, a_in, a_up, w_free, a_free = pieces
    index = lax.axis_index(axis)
    power = lambda k: jnp.exp(-rates * (steps * jnp.asarray(k).astype(jnp.float32)))
    a_both = steps * power(1)
    zeros = jnp.zeros_like(ends)
    incoming, upper = zeros, zeros
    carry = jnp.stack([ends, heads, w_in, a_in, a_up])
    group = jnp.stack([zeros, zeros, w_free, a_free])
    sizes = []
    size = 1
    while size < n:
        sizes.append(size)
        size *= 2
    pairs_of = lambda size: [(i, i ^ size) for i in range(n)]
    carry_partner = lax.ppermute(carry, axis, pairs_of(1)) if sizes else None
    for k, size in enumerate(sizes):
        high = (index // size) % 2 == 1
        f_l, b_l, wa_l, wb_l, wc_l = jnp.where(high, carry_partner, carry)
        f_h, b_h, wa_h, wb_h, wc_h = jnp.where(high, carry, carry_partner)
        step = power(size)
        spread = size * power(size - 1)
        at = index % size
        incoming = incoming + jnp.where(high, power(at) * f_l, 0.0)
        upper = upper + jnp.where(high, 0.0, power(size - 1 - at) * b_h)
        carry = jnp.stack([
            step * f_l + f_h,
            b_l + step * b_h,
            wa_l + step * wa_h,
            wb_l + step * wb_h,
            step * wc_l + wc_h,
        ])
        partner = lax.ppermute(group, axis, pairs_of(size))
        if k + 1 < len(sizes):
            carry_partner = lax.ppermute(carry, axis, pairs_of(sizes[k + 1]))
            partner, carry_partner = lax.optimization_barrier((partner, carry_partner))
        else:
            hidden = hide(incoming, upper)
            partner, hidden = lax.optimization_barrier((partner, hidden))
        low_g = jnp.where(high, partner, group)
        high_g = jnp.where(high, group, partner)
        u_l, v_l, zw_l, za_l = low_g
        u_h, v_h, zw_h, za_h = high_g
        group = jnp.stack([
            step * u_l + (u_h + f_l * spread),
            (v_l + b_h * spread) + step * v_h,
            zw_l + zw_h + f_l * wa_h,
            za_l + za_h + f_l * wb_h + b_h * wc_l + a_both * (b_h * u_l + f_l * v_h),
        ])
    return hidden, group[2], group[3]


def group_sum(x, axis, n, groups):
    for stride, size in levels_of(n, groups):
        x = x + sum(level_gather(x, axis, n, stride, size))
    return x


def local(query_gate, key_gate, value_input, cotangent, residues, decay_rate):
    steps = query_gate.shape[0]
    modes, columns = residues.shape
    peers = lax.axis_size("ctx")
    lanes = lax.axis_size("chan")
    query = query_gate.astype(jnp.float32)
    keyed = key_gate.astype(jnp.float32)
    values = value_input.astype(jnp.float32)
    upstream = cotangent.astype(jnp.float32)
    source = keyed * values
    drive = upstream * query
    decay = jnp.exp(-decay_rate)
    norm_factor = jnp.sqrt(-jnp.expm1(-2.0 * decay_rate))
    mixing = residues * norm_factor

    rate = decay_rate[None]
    where = jnp.arange(steps, dtype=jnp.float32)[:, None, None]
    rising = jnp.exp(rate * where)
    falling = jnp.exp(-rate * where)
    whole = jnp.exp(-decay_rate * steps)

    ends = jnp.sum((jnp.exp(-decay_rate * (steps - 1.0))[None] * rising) * source[:, None, :], axis=0)
    heads = mixing * jnp.sum(falling * drive[:, None, :], axis=0)

    row = jnp.arange(steps)[:, None]
    col = jnp.arange(steps)[None, :]
    lower_tri = (col <= row).astype(jnp.float32)
    upper_tri = (col >= row).astype(jnp.float32)
    flat = (steps, modes * columns)
    climbed = (rising * source[:, None, :]).reshape(flat)
    fallen = (falling * (mixing[None] * drive[:, None, :])).reshape(flat)
    states0 = falling * jnp.dot(lower_tri, climbed, precision=PRECISION).reshape(rising.shape)
    adjoint0 = rising * jnp.dot(upper_tri, fallen, precision=PRECISION).reshape(rising.shape)

    grown = falling * decay[None]
    shrunk = rising * whole[None]
    previous0 = jnp.concatenate([jnp.zeros_like(states0[:1]), states0[:-1]], axis=0)
    w_free = jnp.sum(drive[:, None, :] * states0, axis=0)
    w_in = jnp.sum(drive[:, None, :] * grown, axis=0)
    a_free = jnp.sum(adjoint0 * previous0, axis=0)
    a_in = jnp.sum(adjoint0 * falling, axis=0)
    a_up = jnp.sum(shrunk * previous0, axis=0)
    pieces = (ends, heads, w_in, a_in, a_up, w_free, a_free)

    def finish(incoming, upper):
        states = states0 + grown * incoming[None]
        adjoint = adjoint0 + shrunk * upper[None]
        mixed = jnp.sum(mixing[None] * states, axis=1)
        grad_source = jnp.sum(adjoint, axis=1)
        return (
            (query * mixed).astype(jnp.bfloat16),
            (upstream * mixed).astype(jnp.bfloat16),
            (grad_source * values).astype(jnp.bfloat16),
            (grad_source * keyed).astype(jnp.bfloat16),
        )

    outs, grad_mixing, grad_decay = fused_scan(pieces, decay_rate, steps, "ctx", peers, finish)
    output, grad_query, grad_key, grad_value = outs

    raw_residue = grad_mixing * norm_factor
    raw_lograte = decay_rate * (
        grad_mixing * residues * decay * decay / norm_factor - decay * grad_decay
    )
    part = jnp.sum(raw_residue * raw_residue) + jnp.sum(raw_lograte * raw_lograte)
    total = group_sum(part.reshape(1), "chan", lanes, CHAN_GROUPS)[0]
    limit = math.sqrt(2.0 * MODES * WIDTH)
    scale = jnp.minimum(1.0, limit / jnp.sqrt(total + 1e-06))
    width = columns // peers
    at = lax.axis_index("ctx") * width
    own_residue = lax.dynamic_slice_in_dim(raw_residue, at, width, axis=1)
    own_lograte = lax.dynamic_slice_in_dim(raw_lograte, at, width, axis=1)
    return (output, grad_query, grad_key, grad_value, own_residue * scale, own_lograte * scale)


def solution(mesh):
    placed = (
        P("ctx", "chan"),
        P("ctx", "chan"),
        P("ctx", "chan"),
        P("ctx", "chan"),
        P(None, "chan"),
        P(None, "chan"),
    )
    return jax.shard_map(
        local,
        mesh=mesh,
        in_specs=placed,
        out_specs=(
            P("ctx", "chan"),
            P("ctx", "chan"),
            P("ctx", "chan"),
            P("ctx", "chan"),
            P(None, ("chan", "ctx")),
            P(None, ("chan", "ctx")),
        ),
        check_vma=False,
    )
```

```python
import math

import jax
import jax.numpy as jnp
from jax import lax
from jax.sharding import PartitionSpec as P

WIDTH = 8192
MODES = 16

PRECISION = lax.Precision.HIGH
CTX_GROUPS = (2, 8, 4)
CHAN_GROUPS = (2, 4, 2)


def levels_of(n, groups):
    out, stride = [], 1
    for size in groups:
        out.append((stride, size))
        stride *= size
    assert stride == n
    return out


def level_gather(x, axis, n, stride, size):
    got = []
    for q in range(1, size):
        perm = []
        for i in range(n):
            r = (i // stride) % size
            perm.append((i, i + ((r + q) % size - r) * stride))
        got.append(lax.ppermute(x, axis, perm))
    return got


def fused_scan(pieces, rates, steps, axis, n, hide):
    ends, heads, w_in, a_in, a_up, w_free, a_free = pieces
    index = lax.axis_index(axis)
    power = lambda k: jnp.exp(-rates * (steps * jnp.asarray(k).astype(jnp.float32)))
    a_both = steps * power(1)
    zeros = jnp.zeros_like(ends)
    incoming, upper = zeros, zeros
    carry = jnp.stack([ends, heads])
    group = jnp.stack([w_in, a_in, a_up, zeros, zeros, w_free, a_free])
    sizes = []
    size = 1
    while size < n:
        sizes.append(size)
        size *= 2
    pairs_of = lambda size: [(i, i ^ size) for i in range(n)]
    carry_partner = lax.ppermute(carry, axis, pairs_of(1)) if sizes else None
    for k, size in enumerate(sizes):
        high = (index // size) % 2 == 1
        f_l, b_l = jnp.where(high, carry_partner, carry)
        f_h, b_h = jnp.where(high, carry, carry_partner)
        step = power(size)
        spread = size * power(size - 1)
        at = index % size
        incoming = incoming + jnp.where(high, power(at) * f_l, 0.0)
        upper = upper + jnp.where(high, 0.0, power(size - 1 - at) * b_h)
        carry = jnp.stack([step * f_l + f_h, b_l + step * b_h])
        partner = lax.ppermute(group, axis, pairs_of(size))
        if k + 1 < len(sizes):
            carry_partner = lax.ppermute(carry, axis, pairs_of(sizes[k + 1]))
            partner, carry_partner = lax.optimization_barrier((partner, carry_partner))
        else:
            hidden = hide(incoming, upper)
            partner, hidden = lax.optimization_barrier((partner, hidden))
        low_g = jnp.where(high, partner, group)
        high_g = jnp.where(high, group, partner)
        wa_l, wb_l, wc_l, u_l, v_l, zw_l, za_l = low_g
        wa_h, wb_h, wc_h, u_h, v_h, zw_h, za_h = high_g
        group = jnp.stack([
            wa_l + step * wa_h,
            wb_l + step * wb_h,
            step * wc_l + wc_h,
            step * u_l + (u_h + f_l * spread),
            (v_l + b_h * spread) + step * v_h,
            zw_l + zw_h + f_l * wa_h,
            za_l + za_h + f_l * wb_h + b_h * wc_l + a_both * (b_h * u_l + f_l * v_h),
        ])
    return hidden, group[5], group[6]


def group_sum(x, axis, n, groups):
    for stride, size in levels_of(n, groups):
        x = x + sum(level_gather(x, axis, n, stride, size))
    return x


def local(query_gate, key_gate, value_input, cotangent, residues, decay_rate):
    steps = query_gate.shape[0]
    modes, columns = residues.shape
    peers = lax.axis_size("ctx")
    lanes = lax.axis_size("chan")
    query = query_gate.astype(jnp.float32)
    keyed = key_gate.astype(jnp.float32)
    values = value_input.astype(jnp.float32)
    upstream = cotangent.astype(jnp.float32)
    source = keyed * values
    drive = upstream * query
    decay = jnp.exp(-decay_rate)
    norm_factor = jnp.sqrt(-jnp.expm1(-2.0 * decay_rate))
    mixing = residues * norm_factor

    rate = decay_rate[None]
    where = jnp.arange(steps, dtype=jnp.float32)[:, None, None]
    rising = jnp.exp(rate * where)
    falling = jnp.exp(-rate * where)
    whole = jnp.exp(-decay_rate * steps)

    ends = jnp.sum((jnp.exp(-decay_rate * (steps - 1.0))[None] * rising) * source[:, None, :], axis=0)
    heads = mixing * jnp.sum(falling * drive[:, None, :], axis=0)

    row = jnp.arange(steps)[:, None]
    col = jnp.arange(steps)[None, :]
    lower_tri = (col <= row).astype(jnp.float32)
    upper_tri = (col >= row).astype(jnp.float32)
    flat = (steps, modes * columns)
    climbed = (rising * source[:, None, :]).reshape(flat)
    fallen = (falling * (mixing[None] * drive[:, None, :])).reshape(flat)
    states0 = falling * jnp.dot(lower_tri, climbed, precision=PRECISION).reshape(rising.shape)
    adjoint0 = rising * jnp.dot(upper_tri, fallen, precision=PRECISION).reshape(rising.shape)

    grown = falling * decay[None]
    shrunk = rising * whole[None]
    previous0 = jnp.concatenate([jnp.zeros_like(states0[:1]), states0[:-1]], axis=0)
    w_free = jnp.sum(drive[:, None, :] * states0, axis=0)
    w_in = jnp.sum(drive[:, None, :] * grown, axis=0)
    a_free = jnp.sum(adjoint0 * previous0, axis=0)
    a_in = jnp.sum(adjoint0 * falling, axis=0)
    a_up = jnp.sum(shrunk * previous0, axis=0)
    pieces = (ends, heads, w_in, a_in, a_up, w_free, a_free)

    def finish(incoming, upper):
        states = states0 + grown * incoming[None]
        adjoint = adjoint0 + shrunk * upper[None]
        mixed = jnp.sum(mixing[None] * states, axis=1)
        grad_source = jnp.sum(adjoint, axis=1)
        return (
            (query * mixed).astype(jnp.bfloat16),
            (upstream * mixed).astype(jnp.bfloat16),
            (grad_source * values).astype(jnp.bfloat16),
            (grad_source * keyed).astype(jnp.bfloat16),
        )

    outs, grad_mixing, grad_decay = fused_scan(pieces, decay_rate, steps, "ctx", peers, finish)
    output, grad_query, grad_key, grad_value = outs

    raw_residue = grad_mixing * norm_factor
    raw_lograte = decay_rate * (
        grad_mixing * residues * decay * decay / norm_factor - decay * grad_decay
    )
    part = jnp.sum(raw_residue * raw_residue) + jnp.sum(raw_lograte * raw_lograte)
    total = group_sum(part.reshape(1), "chan", lanes, CHAN_GROUPS)[0]
    limit = math.sqrt(2.0 * MODES * WIDTH)
    scale = jnp.minimum(1.0, limit / jnp.sqrt(total + 1e-06))
    width = columns // peers
    at = lax.axis_index("ctx") * width
    own_residue = lax.dynamic_slice_in_dim(raw_residue, at, width, axis=1)
    own_lograte = lax.dynamic_slice_in_dim(raw_lograte, at, width, axis=1)
    return (output, grad_query, grad_key, grad_value, own_residue * scale, own_lograte * scale)


def solution(mesh):
    placed = (
        P("ctx", "chan"),
        P("ctx", "chan"),
        P("ctx", "chan"),
        P("ctx", "chan"),
        P(None, "chan"),
        P(None, "chan"),
    )
    return jax.shard_map(
        local,
        mesh=mesh,
        in_specs=placed,
        out_specs=(
            P("ctx", "chan"),
            P("ctx", "chan"),
            P("ctx", "chan"),
            P("ctx", "chan"),
            P(None, ("chan", "ctx")),
            P(None, ("chan", "ctx")),
        ),
        check_vma=False,
    )
```

```python
import math

import jax
import jax.numpy as jnp
from jax import lax
from jax.sharding import PartitionSpec as P

WIDTH = 8192
MODES = 16

PRECISION = lax.Precision.HIGH
CTX_GROUPS = (2, 8, 4)
CHAN_GROUPS = (2, 2, 2, 2)


def levels_of(n, groups):
    out, stride = [], 1
    for size in groups:
        out.append((stride, size))
        stride *= size
    assert stride == n
    return out


def level_gather(x, axis, n, stride, size):
    got = []
    for q in range(1, size):
        perm = []
        for i in range(n):
            r = (i // stride) % size
            perm.append((i, i + ((r + q) % size - r) * stride))
        got.append(lax.ppermute(x, axis, perm))
    return got


def fused_scan(pieces, rates, steps, axis, n, hide):
    ends, heads, w_in, a_in, a_up, w_free, a_free = pieces
    index = lax.axis_index(axis)
    power = lambda k: jnp.exp(-rates * (steps * jnp.asarray(k).astype(jnp.float32)))
    a_both = steps * power(1)
    zeros = jnp.zeros_like(ends)
    incoming, upper = zeros, zeros
    carry = jnp.stack([ends, heads])
    group = jnp.stack([w_in, a_in, a_up, zeros, zeros, w_free, a_free])
    sizes = []
    size = 1
    while size < n:
        sizes.append(size)
        size *= 2
    pairs_of = lambda size: [(i, i ^ size) for i in range(n)]
    carry_partner = lax.ppermute(carry, axis, pairs_of(1)) if sizes else None
    for k, size in enumerate(sizes):
        high = (index // size) % 2 == 1
        f_l, b_l = jnp.where(high, carry_partner, carry)
        f_h, b_h = jnp.where(high, carry, carry_partner)
        step = power(size)
        spread = size * power(size - 1)
        at = index % size
        incoming = incoming + jnp.where(high, power(at) * f_l, 0.0)
        upper = upper + jnp.where(high, 0.0, power(size - 1 - at) * b_h)
        carry = jnp.stack([step * f_l + f_h, b_l + step * b_h])
        sent = jnp.concatenate([group[:3], group[5:]]) if k == 0 else group
        partner = lax.ppermute(sent, axis, pairs_of(size))
        if k + 1 < len(sizes):
            carry_partner = lax.ppermute(carry, axis, pairs_of(sizes[k + 1]))
            partner, carry_partner = lax.optimization_barrier((partner, carry_partner))
        else:
            hidden = hide(incoming, upper)
            partner, hidden = lax.optimization_barrier((partner, hidden))
        if k == 0:
            partner = jnp.concatenate([partner[:3], group[3:5], partner[3:]])
        low_g = jnp.where(high, partner, group)
        high_g = jnp.where(high, group, partner)
        wa_l, wb_l, wc_l, u_l, v_l, zw_l, za_l = low_g
        wa_h, wb_h, wc_h, u_h, v_h, zw_h, za_h = high_g
        group = jnp.stack([
            wa_l + step * wa_h,
            wb_l + step * wb_h,
            step * wc_l + wc_h,
            step * u_l + (u_h + f_l * spread),
            (v_l + b_h * spread) + step * v_h,
            zw_l + zw_h + f_l * wa_h,
            za_l + za_h + f_l * wb_h + b_h * wc_l + a_both * (b_h * u_l + f_l * v_h),
        ])
    return hidden, group[5], group[6]


def group_sum(x, axis, n, groups):
    for stride, size in levels_of(n, groups):
        x = x + sum(level_gather(x, axis, n, stride, size))
    return x


def local(query_gate, key_gate, value_input, cotangent, residues, decay_rate):
    steps = query_gate.shape[0]
    modes, columns = residues.shape
    peers = lax.axis_size("ctx")
    lanes = lax.axis_size("chan")
    query = query_gate.astype(jnp.float32)
    keyed = key_gate.astype(jnp.float32)
    values = value_input.astype(jnp.float32)
    upstream = cotangent.astype(jnp.float32)
    source = keyed * values
    drive = upstream * query
    decay = jnp.exp(-decay_rate)
    norm_factor = jnp.sqrt(-jnp.expm1(-2.0 * decay_rate))
    mixing = residues * norm_factor

    rate = decay_rate[None]
    where = jnp.arange(steps, dtype=jnp.float32)[:, None, None]
    rising = jnp.exp(rate * where)
    falling = jnp.exp(-rate * where)
    whole = jnp.exp(-decay_rate * steps)

    ends = jnp.sum((jnp.exp(-decay_rate * (steps - 1.0))[None] * rising) * source[:, None, :], axis=0)
    heads = mixing * jnp.sum(falling * drive[:, None, :], axis=0)

    row = jnp.arange(steps)[:, None]
    col = jnp.arange(steps)[None, :]
    lower_tri = (col <= row).astype(jnp.float32)
    upper_tri = (col >= row).astype(jnp.float32)
    flat = (steps, modes * columns)
    climbed = (rising * source[:, None, :]).reshape(flat)
    fallen = (falling * (mixing[None] * drive[:, None, :])).reshape(flat)
    states0 = falling * jnp.dot(lower_tri, climbed, precision=PRECISION).reshape(rising.shape)
    adjoint0 = rising * jnp.dot(upper_tri, fallen, precision=PRECISION).reshape(rising.shape)

    grown = falling * decay[None]
    shrunk = rising * whole[None]
    previous0 = jnp.concatenate([jnp.zeros_like(states0[:1]), states0[:-1]], axis=0)
    w_free = jnp.sum(drive[:, None, :] * states0, axis=0)
    w_in = jnp.sum(drive[:, None, :] * grown, axis=0)
    a_free = jnp.sum(adjoint0 * previous0, axis=0)
    a_in = jnp.sum(adjoint0 * falling, axis=0)
    a_up = jnp.sum(shrunk * previous0, axis=0)
    pieces = (ends, heads, w_in, a_in, a_up, w_free, a_free)

    def finish(incoming, upper):
        states = states0 + grown * incoming[None]
        adjoint = adjoint0 + shrunk * upper[None]
        mixed = jnp.sum(mixing[None] * states, axis=1)
        grad_source = jnp.sum(adjoint, axis=1)
        return (
            (query * mixed).astype(jnp.bfloat16),
            (upstream * mixed).astype(jnp.bfloat16),
            (grad_source * values).astype(jnp.bfloat16),
            (grad_source * keyed).astype(jnp.bfloat16),
        )

    outs, grad_mixing, grad_decay = fused_scan(pieces, decay_rate, steps, "ctx", peers, finish)
    output, grad_query, grad_key, grad_value = outs

    raw_residue = grad_mixing * norm_factor
    raw_lograte = decay_rate * (
        grad_mixing * residues * decay * decay / norm_factor - decay * grad_decay
    )
    part = jnp.sum(raw_residue * raw_residue) + jnp.sum(raw_lograte * raw_lograte)
    total = group_sum(part.reshape(1), "chan", lanes, CHAN_GROUPS)[0]
    limit = math.sqrt(2.0 * MODES * WIDTH)
    scale = jnp.minimum(1.0, limit / jnp.sqrt(total + 1e-06))
    width = columns // peers
    at = lax.axis_index("ctx") * width
    own_residue = lax.dynamic_slice_in_dim(raw_residue, at, width, axis=1)
    own_lograte = lax.dynamic_slice_in_dim(raw_lograte, at, width, axis=1)
    return (output, grad_query, grad_key, grad_value, own_residue * scale, own_lograte * scale)


def solution(mesh):
    placed = (
        P("ctx", "chan"),
        P("ctx", "chan"),
        P("ctx", "chan"),
        P("ctx", "chan"),
        P(None, "chan"),
        P(None, "chan"),
    )
    return jax.shard_map(
        local,
        mesh=mesh,
        in_specs=placed,
        out_specs=(
            P("ctx", "chan"),
            P("ctx", "chan"),
            P("ctx", "chan"),
            P("ctx", "chan"),
            P(None, ("chan", "ctx")),
            P(None, ("chan", "ctx")),
        ),
        check_vma=False,
    )
```

```python
import math

import jax
import jax.numpy as jnp
from jax import lax
from jax.sharding import PartitionSpec as P

WIDTH = 8192
MODES = 16

PRECISION = lax.Precision.HIGH
CTX_GROUPS = (2, 8, 4)
CHAN_GROUPS = (2, 2, 2, 2)


def levels_of(n, groups):
    out, stride = [], 1
    for size in groups:
        out.append((stride, size))
        stride *= size
    assert stride == n
    return out


def level_gather(x, axis, n, stride, size):
    got = []
    for q in range(1, size):
        perm = []
        for i in range(n):
            r = (i // stride) % size
            perm.append((i, i + ((r + q) % size - r) * stride))
        got.append(lax.ppermute(x, axis, perm))
    return got


def fused_scan(pieces, rates, steps, axis, n, hide):
    ends, heads, w_in, a_in, a_up, w_free, a_free = pieces
    index = lax.axis_index(axis)
    power = lambda k: jnp.exp(-rates * (steps * jnp.asarray(k).astype(jnp.float32)))
    a_both = steps * power(1)
    zeros = jnp.zeros_like(ends)
    incoming, upper = zeros, zeros
    carry = jnp.stack([ends, heads])
    group = jnp.stack([w_in, a_in, a_up, zeros, zeros, w_free, a_free])
    sizes = []
    size = 1
    while size < n:
        sizes.append(size)
        size *= 2
    pairs_of = lambda size: [(i, i ^ size) for i in range(n)]
    carry_partner = lax.ppermute(carry, axis, pairs_of(1)) if sizes else None
    for k, size in enumerate(sizes):
        high = (index // size) % 2 == 1
        f_l, b_l = jnp.where(high, carry_partner, carry)
        f_h, b_h = jnp.where(high, carry, carry_partner)
        step = power(size)
        spread = size * power(size - 1)
        at = index % size
        incoming = incoming + jnp.where(high, power(at) * f_l, 0.0)
        upper = upper + jnp.where(high, 0.0, power(size - 1 - at) * b_h)
        carry = jnp.stack([step * f_l + f_h, b_l + step * b_h])
        partner = lax.ppermute(group, axis, pairs_of(size))
        if k + 1 < len(sizes):
            carry_partner = lax.ppermute(carry, axis, pairs_of(sizes[k + 1]))
            partner, carry_partner = lax.optimization_barrier((partner, carry_partner))
        else:
            hidden = hide(incoming, upper)
            partner, hidden = lax.optimization_barrier((partner, hidden))
        low_g = jnp.where(high, partner, group)
        high_g = jnp.where(high, group, partner)
        wa_l, wb_l, wc_l, u_l, v_l, zw_l, za_l = low_g
        wa_h, wb_h, wc_h, u_h, v_h, zw_h, za_h = high_g
        group = jnp.stack([
            wa_l + step * wa_h,
            wb_l + step * wb_h,
            step * wc_l + wc_h,
            step * u_l + (u_h + f_l * spread),
            (v_l + b_h * spread) + step * v_h,
            zw_l + zw_h + f_l * wa_h,
            za_l + za_h + f_l * wb_h + b_h * wc_l + a_both * (b_h * u_l + f_l * v_h),
        ])
    return hidden, group[5], group[6]


def group_sum(x, axis, n, groups):
    for stride, size in levels_of(n, groups)[::-1]:
        x = x + sum(level_gather(x, axis, n, stride, size))
    return x


def local(query_gate, key_gate, value_input, cotangent, residues, decay_rate):
    steps = query_gate.shape[0]
    modes, columns = residues.shape
    peers = lax.axis_size("ctx")
    lanes = lax.axis_size("chan")
    query = query_gate.astype(jnp.float32)
    keyed = key_gate.astype(jnp.float32)
    values = value_input.astype(jnp.float32)
    upstream = cotangent.astype(jnp.float32)
    source = keyed * values
    drive = upstream * query
    decay = jnp.exp(-decay_rate)
    norm_factor = jnp.sqrt(-jnp.expm1(-2.0 * decay_rate))
    mixing = residues * norm_factor

    rate = decay_rate[None]
    where = jnp.arange(steps, dtype=jnp.float32)[:, None, None]
    rising = jnp.exp(rate * where)
    falling = jnp.exp(-rate * where)
    whole = jnp.exp(-decay_rate * steps)

    ends = jnp.sum((jnp.exp(-decay_rate * (steps - 1.0))[None] * rising) * source[:, None, :], axis=0)
    heads = mixing * jnp.sum(falling * drive[:, None, :], axis=0)

    row = jnp.arange(steps)[:, None]
    col = jnp.arange(steps)[None, :]
    lower_tri = (col <= row).astype(jnp.float32)
    upper_tri = (col >= row).astype(jnp.float32)
    flat = (steps, modes * columns)
    climbed = (rising * source[:, None, :]).reshape(flat)
    fallen = (falling * (mixing[None] * drive[:, None, :])).reshape(flat)
    states0 = falling * jnp.dot(lower_tri, climbed, precision=PRECISION).reshape(rising.shape)
    adjoint0 = rising * jnp.dot(upper_tri, fallen, precision=PRECISION).reshape(rising.shape)

    grown = falling * decay[None]
    shrunk = rising * whole[None]
    previous0 = jnp.concatenate([jnp.zeros_like(states0[:1]), states0[:-1]], axis=0)
    w_free = jnp.sum(drive[:, None, :] * states0, axis=0)
    w_in = jnp.sum(drive[:, None, :] * grown, axis=0)
    a_free = jnp.sum(adjoint0 * previous0, axis=0)
    a_in = jnp.sum(adjoint0 * falling, axis=0)
    a_up = jnp.sum(shrunk * previous0, axis=0)
    pieces = (ends, heads, w_in, a_in, a_up, w_free, a_free)

    def finish(incoming, upper):
        states = states0 + grown * incoming[None]
        adjoint = adjoint0 + shrunk * upper[None]
        mixed = jnp.sum(mixing[None] * states, axis=1)
        grad_source = jnp.sum(adjoint, axis=1)
        return (
            (query * mixed).astype(jnp.bfloat16),
            (upstream * mixed).astype(jnp.bfloat16),
            (grad_source * values).astype(jnp.bfloat16),
            (grad_source * keyed).astype(jnp.bfloat16),
        )

    outs, grad_mixing, grad_decay = fused_scan(pieces, decay_rate, steps, "ctx", peers, finish)
    output, grad_query, grad_key, grad_value = outs

    raw_residue = grad_mixing * norm_factor
    raw_lograte = decay_rate * (
        grad_mixing * residues * decay * decay / norm_factor - decay * grad_decay
    )
    part = jnp.sum(raw_residue * raw_residue) + jnp.sum(raw_lograte * raw_lograte)
    total = group_sum(part.reshape(1), "chan", lanes, CHAN_GROUPS)[0]
    limit = math.sqrt(2.0 * MODES * WIDTH)
    scale = jnp.minimum(1.0, limit / jnp.sqrt(total + 1e-06))
    width = columns // peers
    at = lax.axis_index("ctx") * width
    own_residue = lax.dynamic_slice_in_dim(raw_residue, at, width, axis=1)
    own_lograte = lax.dynamic_slice_in_dim(raw_lograte, at, width, axis=1)
    return (output, grad_query, grad_key, grad_value, own_residue * scale, own_lograte * scale)


def solution(mesh):
    placed = (
        P("ctx", "chan"),
        P("ctx", "chan"),
        P("ctx", "chan"),
        P("ctx", "chan"),
        P(None, "chan"),
        P(None, "chan"),
    )
    return jax.shard_map(
        local,
        mesh=mesh,
        in_specs=placed,
        out_specs=(
            P("ctx", "chan"),
            P("ctx", "chan"),
            P("ctx", "chan"),
            P("ctx", "chan"),
            P(None, ("chan", "ctx")),
            P(None, ("chan", "ctx")),
        ),
        check_vma=False,
    )
```
